1024 devices in a mesh: fsdp: 64 (over z, y_lo), tp: 16 (over x, y_hi, core).
Axes of the slice: x: 4, y: 4 (y_hi: 2, y_lo: 2; y = y_hi * 2 + y_lo), z: 32, core: 2. Of those that a mesh axis runs over, the one named last changes fastest.
Arguments:
- dout: bfloat16 [16384, 4096], P('fsdp', 'tp'), may hold values from -6 to 6
- w_out: bfloat16 [8192, 4096], P(('tp', 'fsdp')), may hold values from -0.09375 to 0.09375
- y_scan: bfloat16 [16384, 8192], P('fsdp', 'tp'), may hold values from -6 to 6
- z_gate: bfloat16 [16384, 8192], P('fsdp', 'tp'), may hold values from -6 to 6
- x_conv: bfloat16 [16384, 8192], P('fsdp', 'tp'), may hold values from -6 to 6
- du_scan: bfloat16 [16384, 8192], P('fsdp', 'tp'), may hold values from -9 to 9
- conv_w: float32 [4, 8192], P(None, 'tp'), may hold values from -3 to 3
- conv_b: float32 [8192], P('tp'), may hold values from -1 to 1
Outputs:
- d_y: bfloat16 [16384, 8192], P('fsdp', 'tp')
- d_z: bfloat16 [16384, 8192], P('fsdp', 'tp')
- d_x: bfloat16 [16384, 8192], P('fsdp', 'tp')
- d_conv_w: float32 [4, 8192], P(None, 'tp')
- d_conv_b: float32 [8192], P('tp')
The draws below stay inside these ranges and needn't reach their ends.
All inputs are finite; a program needn't handle non-finite values.
Results may differ from the reference program's by a relative error of at most 0.001.
Values may be sent and summed in bfloat16 or wider, within the bound.
No kernel may reach another device: no remote copies, remote signals or barrier semaphores. Data moves between devices by JAX's collectives and lax.ppermute only.
A program may use at most 32 MiB of HBM per device.

```python
import jax
import jax.numpy as jnp
from jax import lax

D = 4096
E = 8192
KW = 4
TOK_DEV = 256
TOKENS = 16384
N_TP = 16


def draw_du_scan(key, part):
    position = jnp.arange(TOKENS, dtype=jnp.float32) / (TOKENS - 1)
    ramp = 0.5 + position
    values = jax.random.normal(key, (TOKENS, E), jnp.float32) * ramp[:, None]
    return jnp.clip(values, -9.0, 9.0).astype(jnp.bfloat16)


def shard_levels(stream_key, dims, shards, low, largest):
    factor_of = 1.0
    for dim, blocks in shards:
        draws = jax.random.uniform(jax.random.fold_in(jax.random.fold_in(stream_key, 6), dim), (blocks,), jnp.float32, low / len(shards), largest / len(shards))
        factor_of = factor_of * jnp.repeat(jnp.exp(draws), dims[dim] // blocks).reshape((-1,) + (1,) * (len(dims) - 1 - dim))
    return factor_of


def noise(stream_key, shape, deviation, limit, shards=(), held_as=jnp.bfloat16):
    entries = deviation * jax.random.normal(stream_key, shape, jnp.float32)
    if shards:
        entries = entries * shard_levels(stream_key, shape, shards, -0.22, 0.18)
    return jnp.clip(entries, -limit, limit).astype(held_as)


def setup_inputs(seed: int = 0) -> dict:
    keys = jax.random.split(jax.random.key(seed), 9)
    return {
        "dout": noise(keys[0], (TOKENS, D), 1.0, 6.0, ((0, 64), (1, 16))),
        "w_out": noise(keys[1], (E, D), D ** -0.5, 0.09375, ((0, 1024),)),
        "y_scan": noise(keys[2], (TOKENS, E), 1.0, 6.0, ((0, 64), (1, 16))),
        "z_gate": noise(keys[3], (TOKENS, E), 1.0, 6.0, ((0, 64), (1, 16))),
        "x_conv": noise(keys[4], (TOKENS, E), 1.0, 6.0, ((0, 64), (1, 16))),
        "du_scan": draw_du_scan(jax.random.fold_in(keys[8], 71), 0),
        "conv_w": noise(keys[6], (KW, E), 0.5, 3.0, ((1, 16),), jnp.float32),
        "conv_b": jnp.clip(jax.random.uniform(keys[7], (E,), jnp.float32, -1.0, 1.0) * shard_levels(keys[7], (E,), ((0, 16),), -0.4, 0.0), -1.0, 1.0),
    }


def silu_slope(value):
    sig = jax.nn.sigmoid(value)
    return sig * (1.0 + value * (1.0 - sig))


def reference(dout, w_out, y_scan, z_gate, x_conv, du_scan, conv_w, conv_b):
    nblk = TOKENS // TOK_DEV

    def outer(block):
        d_blk, y_blk, z_blk = block
        d_gated = jnp.dot(d_blk, w_out.T, preferred_element_type=jnp.float32)
        zf = z_blk.astype(jnp.float32)
        grad_y = (d_gated * jax.nn.silu(zf)).astype(jnp.bfloat16)
        grad_z = (d_gated * y_blk.astype(jnp.float32) * silu_slope(zf)).astype(jnp.bfloat16)
        return grad_y, grad_z

    grad_y, grad_z = lax.map(outer, (dout.reshape(nblk, TOK_DEV, D), y_scan.reshape(nblk, TOK_DEV, E), z_gate.reshape(nblk, TOK_DEV, E)))
    grad_y = grad_y.reshape(TOKENS, E)
    grad_z = grad_z.reshape(TOKENS, E)

    width = E // N_TP
    nchan = E // width

    def conv_block(block):
        xb, ub, wb, bb = block
        xpad = jnp.concatenate([jnp.zeros((KW - 1, width), jnp.float32), xb.astype(jnp.float32)], 0)
        pre = jnp.zeros((TOKENS, width), jnp.float32) + bb[None, :]
        for k in range(KW):
            pre = pre + wb[k][None, :] * xpad[k:k + TOKENS]
        d_pre = ub.astype(jnp.float32) * silu_slope(pre)
        dpad = jnp.concatenate([d_pre, jnp.zeros((KW - 1, width), jnp.float32)], 0)
        grad_x = jnp.zeros((TOKENS, width), jnp.float32)
        taps = []
        for k in range(KW):
            grad_x = grad_x + wb[k][None, :] * dpad[KW - 1 - k:KW - 1 - k + TOKENS]
            taps.append(jnp.sum(d_pre * xpad[k:k + TOKENS], 0))
        return grad_x.astype(jnp.bfloat16), jnp.stack(taps), jnp.sum(d_pre, 0)

    xs = x_conv.reshape(TOKENS, nchan, width).transpose(1, 0, 2)
    us = du_scan.reshape(TOKENS, nchan, width).transpose(1, 0, 2)
    ws = conv_w.reshape(KW, nchan, width).transpose(1, 0, 2)
    bs = conv_b.reshape(nchan, width)
    grad_x, grad_w, grad_b = lax.map(conv_block, (xs, us, ws, bs))
    grad_x = grad_x.transpose(1, 0, 2).reshape(TOKENS, E)
    grad_w = grad_w.transpose(1, 0, 2).reshape(KW, E)
    grad_b = grad_b.reshape(E)
    return (grad_y, grad_z, grad_x, grad_w, grad_b)
```

```python
import jax
import jax.numpy as jnp
from jax import lax
from jax.sharding import Mesh
from jax.sharding import PartitionSpec as P

KW = 4
FSDP = ("zh", "zl", "ylo")


def shifted(block, axis, distance):
    devices = range(lax.axis_size(axis))
    route = [(i - distance, i) for i in devices if i - distance in devices]
    return lax.ppermute(block, axis, route)


def silu_slope(value):
    sig = jax.nn.sigmoid(value)
    return sig * (1.0 + value * (1.0 - sig))


def butterfly_sum(value, axis, bits):
    n = lax.axis_size(axis)
    for b in bits:
        value = value + lax.ppermute(value, axis, [(i, i ^ (1 << b)) for i in range(n)])
    return value


def butterfly_gather(block, axis, bits):
    n = lax.axis_size(axis)
    me = lax.axis_index(axis)
    buf = block[None]
    for b in bits:
        recv = lax.ppermute(buf, axis, [(i, i ^ (1 << b)) for i in range(n)])
        bit = (me >> b) & 1
        pair = jnp.zeros((2,) + buf.shape, buf.dtype)
        pair = lax.dynamic_update_slice(pair, buf[None], (bit,) + (0,) * buf.ndim)
        pair = lax.dynamic_update_slice(pair, recv[None], (1 - bit,) + (0,) * buf.ndim)
        buf = pair
    k = len(bits)
    buf = buf.reshape(buf.shape[:k] + block.shape)
    held = [bits[k - 1 - j] for j in range(k)]
    order = sorted(range(k), key=lambda j: -held[j])
    buf = jnp.transpose(buf, order + list(range(k, k + block.ndim)))
    return buf.reshape((n,) + block.shape)


def local(dout, w_out, y_scan, z_gate, x_conv, du_scan, conv_w, conv_b):
    tok_rows = x_conv.shape[0]
    width = x_conv.shape[1]
    prior = shifted(x_conv[tok_rows - (KW - 1) :], FSDP, 1)
    leading = jnp.stack([x_conv[: KW - 1], du_scan[: KW - 1]])
    later = shifted(leading, FSDP, -1)
    extended = jnp.concatenate([prior, x_conv, later[0]], 0)
    span = tok_rows + KW - 1
    pre_all = jnp.zeros((span, width), jnp.float32) + conv_b[None, :]
    for k in range(KW):
        pre_all = pre_all + conv_w[k][None, :] * extended[k : k + span]
    arriving = jnp.concatenate([du_scan, later[1]], 0)
    d_pre_all = arriving.astype(jnp.float32) * silu_slope(pre_all)
    d_pre = d_pre_all[:tok_rows]
    grad_x = jnp.zeros((tok_rows, width), jnp.float32)
    taps = []
    for k in range(KW):
        grad_x = grad_x + conv_w[k][None, :] * d_pre_all[KW - 1 - k : KW - 1 - k + tok_rows]
        taps.append(jnp.sum(d_pre * extended[k : k + tok_rows], 0))
    partial = jnp.concatenate([jnp.stack(taps), jnp.sum(d_pre, 0)[None]], 0)
    fsdp_bits = (lax.axis_size(FSDP) - 1).bit_length()
    total = butterfly_sum(partial, FSDP, list(range(fsdp_bits)))
    grad_w, grad_b = total[:KW], total[KW]
    tp_bits = (lax.axis_size("tp") - 1).bit_length()
    out_blocks = butterfly_gather(dout, "tp", [1] + list(range(tp_bits - 1, 1, -1)) + [0])
    group_w = lax.all_gather(w_out, "ylo", axis=0, tiled=True)
    group_w = lax.all_gather(group_w, "zl", axis=0, tiled=True)
    group_w = lax.all_gather(group_w, "zh", axis=0, tiled=True)
    n_tp = out_blocks.shape[0]
    w_blocks = group_w.reshape(group_w.shape[0], n_tp, dout.shape[1])
    d_gated = lax.dot_general(
        out_blocks, w_blocks, (((0, 2), (1, 2)), ((), ())), preferred_element_type=jnp.float32
    )
    gate_f = z_gate.astype(jnp.float32)
    grad_y = (d_gated * jax.nn.silu(gate_f)).astype(jnp.bfloat16)
    grad_z = (d_gated * y_scan.astype(jnp.float32) * silu_slope(gate_f)).astype(jnp.bfloat16)
    return (grad_y, grad_z, grad_x.astype(jnp.bfloat16), grad_w, grad_b)


def solution(mesh):
    n_f = mesh.shape["fsdp"]
    n_t = mesh.shape["tp"]
    view = Mesh(mesh.devices.reshape(n_f // 4, 2, 2, n_t), FSDP + ("tp",))
    tok = P(FSDP, "tp")
    return jax.shard_map(
        local,
        mesh=view,
        in_specs=(
            tok,
            P(("tp",) + FSDP, None),
            tok,
            tok,
            tok,
            tok,
            P(None, "tp"),
            P("tp"),
        ),
        out_specs=(tok, tok, tok, P(None, "tp"), P("tp")),
        check_vma=False,
    )
```

```python
import jax
import jax.numpy as jnp
from jax import lax
from jax.sharding import Mesh
from jax.sharding import PartitionSpec as P

KW = 4
FSDP = ("zh", "zl", "ylo")


def shifted(block, axis, distance):
    devices = range(lax.axis_size(axis))
    route = [(i - distance, i) for i in devices if i - distance in devices]
    return lax.ppermute(block, axis, route)


def silu_slope(value):
    sig = jax.nn.sigmoid(value)
    return sig * (1.0 + value * (1.0 - sig))


def butterfly_sum(value, axis, bits):
    n = lax.axis_size(axis)
    for b in bits:
        value = value + lax.ppermute(value, axis, [(i, i ^ (1 << b)) for i in range(n)])
    return value


def butterfly_gather(block, axis, bits):
    n = lax.axis_size(axis)
    me = lax.axis_index(axis)
    buf = block[None]
    for b in bits:
        recv = lax.ppermute(buf, axis, [(i, i ^ (1 << b)) for i in range(n)])
        bit = (me >> b) & 1
        pair = jnp.zeros((2,) + buf.shape, buf.dtype)
        pair = lax.dynamic_update_slice(pair, buf[None], (bit,) + (0,) * buf.ndim)
        pair = lax.dynamic_update_slice(pair, recv[None], (1 - bit,) + (0,) * buf.ndim)
        buf = pair
    k = len(bits)
    buf = buf.reshape(buf.shape[:k] + block.shape)
    held = [bits[k - 1 - j] for j in range(k)]
    order = sorted(range(k), key=lambda j: -held[j])
    buf = jnp.transpose(buf, order + list(range(k, k + block.ndim)))
    return buf.reshape((n,) + block.shape)


def local(dout, w_out, y_scan, z_gate, x_conv, du_scan, conv_w, conv_b):
    tok_rows = x_conv.shape[0]
    width = x_conv.shape[1]
    prior = shifted(x_conv[tok_rows - (KW - 1) :], FSDP, 1)
    leading = jnp.stack([x_conv[: KW - 1], du_scan[: KW - 1]])
    later = shifted(leading, FSDP, -1)
    extended = jnp.concatenate([prior, x_conv, later[0]], 0)
    span = tok_rows + KW - 1
    pre_all = jnp.zeros((span, width), jnp.float32) + conv_b[None, :]
    for k in range(KW):
        pre_all = pre_all + conv_w[k][None, :] * extended[k : k + span]
    arriving = jnp.concatenate([du_scan, later[1]], 0)
    d_pre_all = arriving.astype(jnp.float32) * silu_slope(pre_all)
    d_pre = d_pre_all[:tok_rows]
    grad_x = jnp.zeros((tok_rows, width), jnp.float32)
    taps = []
    for k in range(KW):
        grad_x = grad_x + conv_w[k][None, :] * d_pre_all[KW - 1 - k : KW - 1 - k + tok_rows]
        taps.append(jnp.sum(d_pre * extended[k : k + tok_rows], 0))
    partial = jnp.concatenate([jnp.stack(taps), jnp.sum(d_pre, 0)[None]], 0)
    fsdp_bits = (lax.axis_size(FSDP) - 1).bit_length()
    total = butterfly_sum(partial, FSDP, list(range(fsdp_bits)))
    grad_w, grad_b = total[:KW], total[KW]
    tp_bits = (lax.axis_size("tp") - 1).bit_length()
    out_blocks = butterfly_gather(dout, "tp", [1] + list(range(tp_bits - 1, 1, -1)) + [0])
    group_w = lax.all_gather(w_out, "ylo", axis=0, tiled=True)
    group_w = lax.all_gather(group_w, "zl", axis=0, tiled=True)
    group_w = lax.all_gather(group_w, "zh", axis=0, tiled=True)
    full_out = jnp.transpose(out_blocks, (1, 0, 2)).reshape(dout.shape[0], -1)
    d_gated = lax.dot_general(
        full_out, group_w, (((1,), (1,)), ((), ())), preferred_element_type=jnp.float32
    )
    gate_f = z_gate.astype(jnp.float32)
    grad_y = (d_gated * jax.nn.silu(gate_f)).astype(jnp.bfloat16)
    grad_z = (d_gated * y_scan.astype(jnp.float32) * silu_slope(gate_f)).astype(jnp.bfloat16)
    return (grad_y, grad_z, grad_x.astype(jnp.bfloat16), grad_w, grad_b)


def solution(mesh):
    n_f = mesh.shape["fsdp"]
    n_t = mesh.shape["tp"]
    view = Mesh(mesh.devices.reshape(n_f // 4, 2, 2, n_t), FSDP + ("tp",))
    tok = P(FSDP, "tp")
    return jax.shard_map(
        local,
        mesh=view,
        in_specs=(
            tok,
            P(("tp",) + FSDP, None),
            tok,
            tok,
            tok,
            tok,
            P(None, "tp"),
            P("tp"),
        ),
        out_specs=(tok, tok, tok, P(None, "tp"), P("tp")),
        check_vma=False,
    )
```

```python
import jax
import jax.numpy as jnp
from jax import lax
from jax.sharding import Mesh
from jax.sharding import PartitionSpec as P

KW = 4
FSDP = ("zh", "zl", "ylo")


def shifted(block, axis, distance):
    devices = range(lax.axis_size(axis))
    route = [(i - distance, i) for i in devices if i - distance in devices]
    return lax.ppermute(block, axis, route)


def silu_slope(value):
    sig = jax.nn.sigmoid(value)
    return sig * (1.0 + value * (1.0 - sig))


def butterfly_sum(value, axis, bits):
    n = lax.axis_size(axis)
    for b in bits:
        value = value + lax.ppermute(value, axis, [(i, i ^ (1 << b)) for i in range(n)])
    return value


def butterfly_gather(block, axis, bits):
    n = lax.axis_size(axis)
    me = lax.axis_index(axis)
    buf = block[None]
    for b in bits:
        recv = lax.ppermute(buf, axis, [(i, i ^ (1 << b)) for i in range(n)])
        bit = (me >> b) & 1
        pair = jnp.zeros((2,) + buf.shape, buf.dtype)
        pair = lax.dynamic_update_slice(pair, buf[None], (bit,) + (0,) * buf.ndim)
        pair = lax.dynamic_update_slice(pair, recv[None], (1 - bit,) + (0,) * buf.ndim)
        buf = pair
    k = len(bits)
    buf = buf.reshape(buf.shape[:k] + block.shape)
    held = [bits[k - 1 - j] for j in range(k)]
    order = sorted(range(k), key=lambda j: -held[j])
    buf = jnp.transpose(buf, order + list(range(k, k + block.ndim)))
    return buf.reshape((n,) + block.shape)


def local(dout, w_out, y_scan, z_gate, x_conv, du_scan, conv_w, conv_b):
    tok_rows = x_conv.shape[0]
    width = x_conv.shape[1]
    prior = shifted(x_conv[tok_rows - (KW - 1) :], FSDP, 1)
    leading = jnp.stack([x_conv[: KW - 1], du_scan[: KW - 1]])
    later = shifted(leading, FSDP, -1)
    extended = jnp.concatenate([prior, x_conv, later[0]], 0)
    span = tok_rows + KW - 1
    pre_all = jnp.zeros((span, width), jnp.float32) + conv_b[None, :]
    for k in range(KW):
        pre_all = pre_all + conv_w[k][None, :] * extended[k : k + span]
    arriving = jnp.concatenate([du_scan, later[1]], 0)
    d_pre_all = arriving.astype(jnp.float32) * silu_slope(pre_all)
    d_pre = d_pre_all[:tok_rows]
    grad_x = jnp.zeros((tok_rows, width), jnp.float32)
    taps = []
    for k in range(KW):
        grad_x = grad_x + conv_w[k][None, :] * d_pre_all[KW - 1 - k : KW - 1 - k + tok_rows]
        taps.append(jnp.sum(d_pre * extended[k : k + tok_rows], 0))
    partial = jnp.concatenate([jnp.stack(taps), jnp.sum(d_pre, 0)[None]], 0)
    fsdp_bits = (lax.axis_size(FSDP) - 1).bit_length()
    total = butterfly_sum(partial, FSDP, list(range(fsdp_bits)))
    grad_w, grad_b = total[:KW], total[KW]
    gate_f = z_gate.astype(jnp.float32)
    y_factor = jax.nn.silu(gate_f)
    z_factor = y_scan.astype(jnp.float32) * silu_slope(gate_f)
    y_factor, z_factor = lax.optimization_barrier((y_factor, z_factor))
    tp_bits = (lax.axis_size("tp") - 1).bit_length()
    out_blocks = butterfly_gather(dout, "tp", [1] + list(range(tp_bits - 1, 1, -1)) + [0])
    group_w = lax.all_gather(w_out, "ylo", axis=0, tiled=True)
    group_w = lax.all_gather(group_w, "zl", axis=0, tiled=True)
    group_w = lax.all_gather(group_w, "zh", axis=0, tiled=True)
    full_out = jnp.transpose(out_blocks, (1, 0, 2)).reshape(dout.shape[0], -1)
    d_gated = lax.dot_general(
        full_out, group_w, (((1,), (1,)), ((), ())), preferred_element_type=jnp.float32
    )
    grad_y = (d_gated * y_factor).astype(jnp.bfloat16)
    grad_z = (d_gated * z_factor).astype(jnp.bfloat16)
    return (grad_y, grad_z, grad_x.astype(jnp.bfloat16), grad_w, grad_b)


def solution(mesh):
    n_f = mesh.shape["fsdp"]
    n_t = mesh.shape["tp"]
    view = Mesh(mesh.devices.reshape(n_f // 4, 2, 2, n_t), FSDP + ("tp",))
    tok = P(FSDP, "tp")
    return jax.shard_map(
        local,
        mesh=view,
        in_specs=(
            tok,
            P(("tp",) + FSDP, None),
            tok,
            tok,
            tok,
            tok,
            P(None, "tp"),
            P("tp"),
        ),
        out_specs=(tok, tok, tok, P(None, "tp"), P("tp")),
        check_vma=False,
    )
```

```python
import jax
import jax.numpy as jnp
from jax import lax
from jax.sharding import Mesh
from jax.sharding import PartitionSpec as P

KW = 4
FSDP = ("zh", "zl", "ylo")


def shifted(block, axis, distance):
    devices = range(lax.axis_size(axis))
    route = [(i - distance, i) for i in devices if i - distance in devices]
    return lax.ppermute(block, axis, route)


def silu_slope(value):
    sig = jax.nn.sigmoid(value)
    return sig * (1.0 + value * (1.0 - sig))


def butterfly_sum(value, axis, bits):
    n = lax.axis_size(axis)
    for b in bits:
        value = value + lax.ppermute(value, axis, [(i, i ^ (1 << b)) for i in range(n)])
    return value


def butterfly_gather(block, axis, bits):
    n = lax.axis_size(axis)
    me = lax.axis_index(axis)
    buf = block[None]
    for b in bits:
        recv = lax.ppermute(buf, axis, [(i, i ^ (1 << b)) for i in range(n)])
        bit = (me >> b) & 1
        pair = jnp.zeros((2,) + buf.shape, buf.dtype)
        pair = lax.dynamic_update_slice(pair, buf[None], (bit,) + (0,) * buf.ndim)
        pair = lax.dynamic_update_slice(pair, recv[None], (1 - bit,) + (0,) * buf.ndim)
        buf = pair
    k = len(bits)
    buf = buf.reshape(buf.shape[:k] + block.shape)
    held = [bits[k - 1 - j] for j in range(k)]
    order = sorted(range(k), key=lambda j: -held[j])
    buf = jnp.transpose(buf, order + list(range(k, k + block.ndim)))
    return buf.reshape((n,) + block.shape)


def local(dout, w_out, y_scan, z_gate, x_conv, du_scan, conv_w, conv_b):
    tok_rows = x_conv.shape[0]
    width = x_conv.shape[1]
    prior = shifted(x_conv[tok_rows - (KW - 1) :], FSDP, 1)
    leading = jnp.stack([x_conv[: KW - 1], du_scan[: KW - 1]])
    later = shifted(leading, FSDP, -1)
    extended = jnp.concatenate([prior, x_conv, later[0]], 0)
    span = tok_rows + KW - 1
    pre_all = jnp.zeros((span, width), jnp.float32) + conv_b[None, :]
    for k in range(KW):
        pre_all = pre_all + conv_w[k][None, :] * extended[k : k + span]
    arriving = jnp.concatenate([du_scan, later[1]], 0)
    d_pre_all = arriving.astype(jnp.float32) * silu_slope(pre_all)
    d_pre = d_pre_all[:tok_rows]
    grad_x = jnp.zeros((tok_rows, width), jnp.float32)
    taps = []
    for k in range(KW):
        grad_x = grad_x + conv_w[k][None, :] * d_pre_all[KW - 1 - k : KW - 1 - k + tok_rows]
        taps.append(jnp.sum(d_pre * extended[k : k + tok_rows], 0))
    partial = jnp.concatenate([jnp.stack(taps), jnp.sum(d_pre, 0)[None]], 0)
    fsdp_bits = (lax.axis_size(FSDP) - 1).bit_length()
    total = butterfly_sum(partial, FSDP, list(range(fsdp_bits)))
    grad_w, grad_b = total[:KW], total[KW]
    tp_bits = (lax.axis_size("tp") - 1).bit_length()
    out_blocks = butterfly_gather(dout, "tp", [1] + list(range(tp_bits - 1, 1, -1)) + [0])
    group_w = lax.all_gather(w_out, ("zl", "ylo"), axis=0, tiled=True)
    group_w = lax.all_gather(group_w, "zh", axis=0, tiled=True)
    full_out = jnp.transpose(out_blocks, (1, 0, 2)).reshape(dout.shape[0], -1)
    d_gated = lax.dot_general(
        full_out, group_w, (((1,), (1,)), ((), ())), preferred_element_type=jnp.float32
    )
    gate_f = z_gate.astype(jnp.float32)
    grad_y = (d_gated * jax.nn.silu(gate_f)).astype(jnp.bfloat16)
    grad_z = (d_gated * y_scan.astype(jnp.float32) * silu_slope(gate_f)).astype(jnp.bfloat16)
    return (grad_y, grad_z, grad_x.astype(jnp.bfloat16), grad_w, grad_b)


def solution(mesh):
    n_f = mesh.shape["fsdp"]
    n_t = mesh.shape["tp"]
    view = Mesh(mesh.devices.reshape(n_f // 4, 2, 2, n_t), FSDP + ("tp",))
    tok = P(FSDP, "tp")
    return jax.shard_map(
        local,
        mesh=view,
        in_specs=(
            tok,
            P(("tp",) + FSDP, None),
            tok,
            tok,
            tok,
            tok,
            P(None, "tp"),
            P("tp"),
        ),
        out_specs=(tok, tok, tok, P(None, "tp"), P("tp")),
        check_vma=False,
    )
```
